128 devices in a mesh: expert: 32 (over y, x, core), dp: 4 (over z).
Axes of the slice: x: 4, y: 4, z: 4, core: 2. Of those that a mesh axis runs over, the one named last changes fastest.
Arguments:
- tokens: bfloat16 [16384, 2048], P(('expert', 'dp')), may hold values from -6 to 6
- expert_ids: int32 [16384, 8], P(('expert', 'dp')), may hold values from 0 to 63, all different within a row; in each aligned block of 128 rows (0 to 127, 128 to 255, ...) at most 20 rows name the same one
- gate_probs: float32 [16384, 8], P(('expert', 'dp')), may hold values from 0.02 to 0.4
- cotangent: bfloat16 [16384, 2048], P(('expert', 'dp')), may hold values from -6 to 6
- weight_in: bfloat16 [64, 2048, 768], P('expert'), may hold values from -0.125 to 0.125
- weight_down: bfloat16 [64, 384, 2048], P('expert'), may hold values from -0.3125 to 0.3125
- swap_flag: int32 [32], replicated, may hold values from 0 to 1, as said below
Outputs:
- layer_out: bfloat16 [16384, 2048], P(('expert', 'dp'))
- gate_grads: float32 [16384, 8], P(('expert', 'dp'))
- token_grads: bfloat16 [16384, 2048], P(('expert', 'dp'))
- grad_in: float32 [64, 2048, 768], P('expert', 'dp')
- grad_down: float32 [64, 384, 2048], P('expert', None, 'dp')
The draws below stay inside these ranges and needn't reach their ends.
Inputs may be any that keep to these rules, and one draw needn't show every extreme that they name: `expert_ids`: each row names 8 different experts. Among the 128 rows of one device no expert is named more than 20 times, and in some of these aligned blocks an expert is named exactly 20 times. swap_flag[i] = swap_flag[i XOR 2]. Where swap_flag[i] is 1, index i of the expert axis takes over the 2 experts of index i XOR 2; experts j * 2 to (j + 1) * 2 - 1 start on index j.
All inputs are finite; a program needn't handle non-finite values.
Results may differ from the reference program's by a relative error of at most 0.0085.
Values may be sent and summed in bfloat16 or wider, within the bound.
No kernel may reach another device: no remote copies, remote signals or barrier semaphores. Data moves between devices by JAX's collectives and lax.ppermute only.
A program may use at most 128 MiB of HBM per device.

```python
import math
import jax
import jax.numpy as jnp
import numpy as np
from jax import lax

D = 2048
FF = 384
EXPERTS = 64
TOP = 8
TOK_DEV = 128
CAP = 20
EXP_DEV = 2
TOKENS = 16384
N_EXPERT = 32
N_DP = 4


def draw_swap_flag(key, part):
    raw_flags = jax.random.randint(key, (N_EXPERT,), 0, 2, dtype=jnp.int32)
    raw_flags = raw_flags.at[0].set(1).at[1].set(0)
    positions = jnp.arange(N_EXPERT, dtype=jnp.int32)
    partner = jnp.bitwise_xor(positions, 2)
    return raw_flags[jnp.minimum(positions, partner)]


def shard_levels(stream_key, dims, shards, least, top_value):
    def one(position, blocks):
        heights = jax.random.uniform(jax.random.fold_in(jax.random.fold_in(stream_key, 6), position), (blocks,), jnp.float32, least / len(shards), top_value / len(shards))
        return jnp.repeat(jnp.exp(heights), dims[position] // blocks).reshape((-1,) + (1,) * (len(dims) - position - 1))

    level = one(*shards[0])
    for cut in shards[1:]:
        level = level * one(*cut)
    return level


def shared_out(rng, own, number, rows, count, top, limit, skew):
    sequence = jax.random.permutation(rng, count)
    heavy_load, usual = load_shares(count, rows * top, limit, skew, True), load_shares(count, rows * top, limit, skew, False)
    places = jnp.arange(count)

    def named(lengths, offset_by):
        used = int((lengths > 0).sum())
        fixed = max(1, used // 4)
        shifted = fixed + (places - fixed + offset_by * (used - fixed)) % max(1, count - fixed)
        return jnp.zeros((count,), jnp.int32).at[sequence[jnp.where(places < fixed, places, shifted)]].set(jnp.asarray(lengths, jnp.int32))

    lengths = jnp.where(number % 4 == 0, named(heavy_load, number // 4), named(usual, number - number // 4 - 1))
    mixed = jax.random.permutation(jax.random.fold_in(own, 3), count)
    source_of, receiver = mixed[0:count // 2 * 2:2], mixed[1:count // 2 * 2:2]
    room = jnp.minimum(lengths[source_of] - 1, limit - lengths[receiver]) // 2
    room = jnp.where((source_of == sequence[0]) | (receiver == sequence[0]) | (lengths[receiver] == 0), 0, jnp.maximum(room, 0))
    shifted = jax.random.randint(jax.random.fold_in(own, 4), (count // 2,), 0, 1 << 20) % (room + 1)
    lengths = lengths.at[source_of].add(-shifted).at[receiver].add(shifted)
    labels = jnp.searchsorted(jnp.cumsum(lengths), jnp.arange(rows * top), side="right").astype(jnp.int32)
    listing = labels.reshape(top, rows).T
    listing = listing[jax.random.permutation(jax.random.fold_in(own, 1), rows)]
    offset_by = jax.random.randint(jax.random.fold_in(own, 2), (rows, 1), 0, top)
    return jnp.take_along_axis(listing, (jnp.arange(top)[None, :] + offset_by) % top, axis=1)


def load_shares(count, total, bound, slope, full):
    weights = [(1 << 20) // math.isqrt(rank ** slope) + 1 for rank in range(1, count + 1)]
    largest = bound if full else min(bound, max(-(-total // count), total * weights[0] // sum(weights)))
    least = 1 if total - largest >= count - 1 else 0
    holding, rest = [largest] + [least] * (count - 1), total - largest - least * (count - 1)
    while rest > 0:
        free = [i for i in range(1, count) if holding[i] < largest] or [i for i in range(1, count) if holding[i] < bound]
        pool, budget = sum([weights[i] for i in free]), rest
        for i in free:
            extra = min(bound - holding[i], max(1, budget * weights[i] // pool), rest)
            holding[i] = holding[i] + extra
            rest = rest - extra
    return np.array(holding)


def bell_draw(own_key, shape, scale, bound, pieces=(), kind=jnp.bfloat16):
    array = jax.random.normal(own_key, shape, jnp.float32) * scale
    if len(pieces) > 0:
        array = shard_levels(own_key, shape, pieces, -0.22, 0.18) * array
    return jnp.clip(array, min=-bound, max=bound).astype(kind)


def setup_inputs(seed: int = 0) -> dict:
    seeds = jax.random.split(jax.random.key(seed), 8)
    tokens = bell_draw(seeds[0], (TOKENS, D), 1.0, 6.0, ((0, 128),))
    expert_ids_keys = jax.random.split(jax.random.fold_in(seeds[1], 1), TOKENS // TOK_DEV)
    expert_ids_turns = jax.random.permutation(jax.random.fold_in(seeds[1], 3), TOKENS // TOK_DEV)
    expert_ids = jax.vmap(lambda own, number: shared_out(jax.random.fold_in(seeds[1], 2), own, number, TOK_DEV, EXPERTS, TOP, CAP, 2))(expert_ids_keys, expert_ids_turns).reshape((TOKENS, TOP))
    gate_probs = jnp.clip(jnp.exp(math.log(0.4) - 2.9957323 * jax.random.uniform(seeds[2], (TOKENS, TOP), jnp.float32) ** shard_levels(seeds[2], (TOKENS, TOP), ((0, 128),), -0.2, 0.2)), 0.02, 0.4)
    cotangent = bell_draw(seeds[3], (TOKENS, D), 1.0, 6.0, ((0, 128),))
    weight_in = bell_draw(seeds[4], (EXPERTS, D, 2 * FF), D ** -0.5, 0.125, ((0, 32),))
    weight_down = bell_draw(seeds[5], (EXPERTS, FF, D), FF ** -0.5, 0.3125, ((0, 32),))
    swap_flag = draw_swap_flag(jax.random.fold_in(seeds[7], 71), 0)
    return dict(tokens=tokens, expert_ids=expert_ids, gate_probs=gate_probs, cotangent=cotangent, weight_in=weight_in, weight_down=weight_down, swap_flag=swap_flag)


def expert_pass(rows_x, rows_grad, first_weight, second_weight):
    projected = jnp.dot(rows_x, first_weight, preferred_element_type=jnp.float32)
    width = second_weight.shape[0]
    pre_gate = projected[:, :width]
    up_part = projected[:, width:]
    sigmoid_gate = jax.nn.sigmoid(pre_gate)
    activated = pre_gate * sigmoid_gate
    hidden = (activated * up_part).astype(jnp.bfloat16)
    expert_out = jnp.dot(hidden, second_weight, preferred_element_type=jnp.float32).astype(jnp.bfloat16)
    hidden_grad = jnp.dot(rows_grad, second_weight.T, preferred_element_type=jnp.float32)
    gate_grad = hidden_grad * up_part * sigmoid_gate * (1.0 + pre_gate * (1.0 - sigmoid_gate))
    proj_grad = jnp.concatenate([gate_grad, hidden_grad * activated], axis=-1).astype(jnp.bfloat16)
    row_grad = jnp.dot(proj_grad, first_weight.T, preferred_element_type=jnp.float32).astype(jnp.bfloat16)
    return hidden, expert_out, proj_grad, row_grad


def reference(tokens, expert_ids, gate_probs, cotangent, weight_in, weight_down, swap_flag):
    assigned = TOKENS * TOP
    blocks = N_EXPERT * N_DP
    flat_ids = expert_ids.reshape(-1).astype(jnp.int32)
    onehot = (flat_ids[:, None] == jnp.arange(EXPERTS, dtype=jnp.int32)[None, :]).astype(jnp.int32)
    onehot = onehot.reshape(blocks, TOK_DEV * TOP, EXPERTS)
    earlier = jnp.cumsum(onehot, axis=1) - onehot
    slot_rank = jnp.sum(earlier * onehot, axis=2).reshape(-1).astype(jnp.int32)
    block_of = (jnp.arange(assigned, dtype=jnp.int32) // (TOK_DEV * TOP)).astype(jnp.int32)
    slot_index = (flat_ids * (blocks * CAP) + block_of * CAP + slot_rank).astype(jnp.int32)
    table = jnp.full((EXPERTS * blocks * CAP,), assigned, jnp.int32)
    table = table.at[slot_index].set(jnp.arange(assigned, dtype=jnp.int32))
    table = table.reshape(EXPERTS, blocks * CAP)
    tokens_pad = jnp.concatenate([tokens, jnp.zeros((1, D), tokens.dtype)], axis=0)
    cot_pad = jnp.concatenate([cotangent, jnp.zeros((1, D), cotangent.dtype)], axis=0)
    probs_pad = jnp.concatenate([gate_probs.reshape(-1), jnp.zeros((1,), gate_probs.dtype)])

    def per_expert(carry, inputs):
        layer_acc, grad_acc, gate_acc = carry
        rows, first_weight, second_weight = inputs
        token_of = (rows // TOP).astype(jnp.int32)
        rows_x = tokens_pad[token_of]
        rows_prob = probs_pad[rows]
        rows_cot = cot_pad[token_of].astype(jnp.float32)
        rows_grad = (rows_prob[:, None] * rows_cot).astype(jnp.bfloat16)
        hidden, expert_out, proj_grad, row_grad = expert_pass(rows_x, rows_grad, first_weight, second_weight)
        out_wide = expert_out.astype(jnp.float32)
        layer_acc = layer_acc.at[token_of].add(rows_prob[:, None] * out_wide)
        grad_acc = grad_acc.at[token_of].add(row_grad.astype(jnp.float32))
        gate_acc = gate_acc.at[rows].set(jnp.sum(rows_cot * out_wide, axis=1))
        x_four = rows_x.reshape(N_EXPERT, N_DP, CAP, D).astype(jnp.float32)
        pg_four = proj_grad.reshape(N_EXPERT, N_DP, CAP, 2 * FF).astype(jnp.float32)
        hid_four = hidden.reshape(N_EXPERT, N_DP, CAP, FF).astype(jnp.float32)
        og_four = rows_grad.reshape(N_EXPERT, N_DP, CAP, D).astype(jnp.float32)
        replica_in = jnp.einsum('idcx,idcf->dxf', x_four, pg_four, precision=lax.Precision.HIGHEST)
        replica_down = jnp.einsum('idcf,idcx->dfx', hid_four, og_four, precision=lax.Precision.HIGHEST)
        replica_in = lax.optimization_barrier(replica_in.astype(jnp.bfloat16))
        replica_down = lax.optimization_barrier(replica_down.astype(jnp.bfloat16))
        summed_in = jnp.sum(replica_in.astype(jnp.float32), axis=0)
        summed_down = jnp.sum(replica_down.astype(jnp.float32), axis=0)
        return (layer_acc, grad_acc, gate_acc), (summed_in, summed_down)

    start = (jnp.zeros((TOKENS + 1, D), jnp.float32), jnp.zeros((TOKENS + 1, D), jnp.float32), jnp.zeros((assigned + 1,), jnp.float32))
    finals, stacked = lax.scan(per_expert, start, (table, weight_in, weight_down))
    layer_acc, grad_acc, gate_acc = finals
    grads_in, grads_down = stacked
    layer_out = layer_acc[:TOKENS].astype(jnp.bfloat16)
    token_grads = grad_acc[:TOKENS].astype(jnp.bfloat16)
    gate_grads = gate_acc[:assigned].reshape(TOKENS, TOP)
    slot_ids = jnp.arange(EXPERTS, dtype=jnp.int32)
    device_of = (slot_ids // EXP_DEV).astype(jnp.int32)
    moved = swap_flag.astype(jnp.int32)[device_of]
    held_expert = (jnp.bitwise_xor(device_of, 2 * moved) * EXP_DEV + slot_ids % EXP_DEV).astype(jnp.int32)
    return layer_out, gate_grads, token_grads, grads_in[held_expert], grads_down[held_expert]
```

```python
import jax
import jax.numpy as jnp
from jax import lax
from jax.sharding import PartitionSpec as P

FF = 384
TOP = 8
CAP = 20


def swapped(block, axis, apart):
    count = lax.axis_size(axis)
    route = []
    for low in range(count):
        high = low | 1 << apart
        if high != low and high < count:
            route += [(low, high), (high, low)]
    return lax.ppermute(block, axis, route)


def body(tokens, expert_ids, gate_probs, cotangent, weight_in, weight_down, swap_flag):
    row_count = tokens.shape[0]
    model_width = tokens.shape[1]
    per_device = weight_in.shape[0]
    groups = lax.axis_size("expert")
    experts = groups * per_device
    device_ids = jnp.arange(groups, dtype=jnp.int32)
    my_index = lax.axis_index("expert")
    my_flag = jnp.sum(jnp.where(device_ids == my_index, swap_flag, 0))
    expert_range = jnp.arange(experts, dtype=jnp.int32)
    chosen = expert_ids[:, :, None] == expert_range[None, None, :]
    member = jnp.any(chosen, axis=1)
    row_range = jnp.arange(row_count, dtype=jnp.int32)
    lower = (row_range[:, None] > row_range[None, :]).astype(jnp.bfloat16)
    earlier = jnp.dot(lower, member.astype(jnp.bfloat16), preferred_element_type=jnp.float32)
    rank = earlier.astype(jnp.int32)
    slot_hit = member[:, :, None] & (rank[:, :, None] == jnp.arange(CAP, dtype=jnp.int32)[None, None, :])
    gather_rows = slot_hit.reshape(row_count, experts * CAP).astype(jnp.bfloat16)
    prob_of = jnp.sum(jnp.where(chosen, gate_probs[:, :, None], 0.0), axis=1)
    slot_prob = jnp.sum(jnp.where(slot_hit, prob_of[:, :, None], 0.0), axis=0).reshape(experts * CAP)
    send_x = jnp.dot(gather_rows.T, tokens, preferred_element_type=jnp.float32).astype(jnp.bfloat16)
    send_c = jnp.dot(gather_rows.T, cotangent, preferred_element_type=jnp.float32)
    send_grad = (slot_prob[:, None] * send_c).astype(jnp.bfloat16)
    send_x = send_x.reshape(groups, per_device, CAP, model_width)
    send_grad = send_grad.reshape(groups, per_device, CAP, model_width)
    recv_x = lax.all_to_all(send_x, "expert", split_axis=0, concat_axis=0, tiled=True)
    recv_grad = lax.all_to_all(send_grad, "expert", split_axis=0, concat_axis=0, tiled=True)
    projected = jnp.einsum("nscd,sdf->nscf", recv_x, weight_in, preferred_element_type=jnp.float32)
    pre_gate = projected[..., :FF]
    up_part = projected[..., FF:]
    sigmoid_gate = jax.nn.sigmoid(pre_gate)
    activated = pre_gate * sigmoid_gate
    hidden = (activated * up_part).astype(jnp.bfloat16)
    expert_out = jnp.einsum(
        "nscf,sfd->nscd", hidden, weight_down, preferred_element_type=jnp.float32
    ).astype(jnp.bfloat16)
    home_out = lax.all_to_all(expert_out, "expert", split_axis=0, concat_axis=0, tiled=True)
    hidden_grad = jnp.einsum(
        "nscd,sfd->nscf", recv_grad, weight_down, preferred_element_type=jnp.float32
    )
    gate_grad = hidden_grad * up_part * sigmoid_gate * (1.0 + pre_gate * (1.0 - sigmoid_gate))
    proj_grad = jnp.concatenate([gate_grad, hidden_grad * activated], axis=-1).astype(jnp.bfloat16)
    row_grad = jnp.einsum(
        "nscf,sdf->nscd", proj_grad, weight_in, preferred_element_type=jnp.float32
    ).astype(jnp.bfloat16)
    home_grad = lax.all_to_all(row_grad, "expert", split_axis=0, concat_axis=0, tiled=True)
    grad_first = jnp.einsum("nscd,nscf->sdf", recv_x, proj_grad, preferred_element_type=jnp.float32)
    grad_second = jnp.einsum(
        "nscf,nscd->sfd", hidden, recv_grad, preferred_element_type=jnp.float32
    )
    reduced_in = lax.psum_scatter(
        grad_first.astype(jnp.bfloat16), "dp", scatter_dimension=1, tiled=True
    )
    reduced_down = lax.psum_scatter(
        grad_second.astype(jnp.bfloat16), "dp", scatter_dimension=2, tiled=True
    )
    partner_in, partner_down = swapped((reduced_in, reduced_down), "expert", 1)
    held_in = jnp.where(my_flag == 1, partner_in, reduced_in).astype(jnp.float32)
    held_down = jnp.where(my_flag == 1, partner_down, reduced_down).astype(jnp.float32)
    out_rows = home_out.reshape(experts * CAP, model_width)
    back_rows = home_grad.reshape(experts * CAP, model_width)
    combine = jnp.where(slot_hit, prob_of[:, :, None], 0.0).reshape(row_count, experts * CAP)
    layer_out = jnp.dot(
        combine, out_rows.astype(jnp.float32), precision=lax.Precision.HIGHEST,
        preferred_element_type=jnp.float32,
    ).astype(jnp.bfloat16)
    scores = jnp.dot(cotangent, out_rows.T, preferred_element_type=jnp.float32)
    rank_of = jnp.sum(jnp.where(chosen, rank[:, None, :], 0), axis=2)
    slot_of = expert_ids * CAP + rank_of
    gate_grads = jnp.take_along_axis(scores, slot_of, axis=1)
    token_grads = jnp.dot(gather_rows, back_rows, preferred_element_type=jnp.float32).astype(
        jnp.bfloat16
    )
    return (layer_out, gate_grads, token_grads, held_in, held_down)


def solution(mesh):
    in_specs = (
        P(("expert", "dp"), None),
        P(("expert", "dp"), None),
        P(("expert", "dp"), None),
        P(("expert", "dp"), None),
        P("expert", None, None),
        P("expert", None, None),
        P(),
    )
    out_specs = (
        P(("expert", "dp"), None),
        P(("expert", "dp"), None),
        P(("expert", "dp"), None),
        P("expert", "dp", None),
        P("expert", None, "dp"),
    )
    return jax.shard_map(body, mesh=mesh, in_specs=in_specs, out_specs=out_specs, check_vma=False)
```

```python
import jax
import jax.numpy as jnp
from jax import lax
from jax.sharding import PartitionSpec as P

FF = 384
TOP = 8
CAP = 20


def swapped(block, axis, apart):
    count = lax.axis_size(axis)
    route = []
    for low in range(count):
        high = low | 1 << apart
        if high != low and high < count:
            route += [(low, high), (high, low)]
    return lax.ppermute(block, axis, route)


def body(tokens, expert_ids, gate_probs, cotangent, weight_in, weight_down, swap_flag):
    row_count = tokens.shape[0]
    model_width = tokens.shape[1]
    per_device = weight_in.shape[0]
    groups = lax.axis_size("expert")
    experts = groups * per_device
    device_ids = jnp.arange(groups, dtype=jnp.int32)
    my_index = lax.axis_index("expert")
    my_flag = jnp.sum(jnp.where(device_ids == my_index, swap_flag, 0))
    expert_range = jnp.arange(experts, dtype=jnp.int32)
    chosen = expert_ids[:, :, None] == expert_range[None, None, :]
    member = jnp.any(chosen, axis=1)
    row_range = jnp.arange(row_count, dtype=jnp.int32)
    lower = (row_range[:, None] > row_range[None, :]).astype(jnp.bfloat16)
    earlier = jnp.dot(lower, member.astype(jnp.bfloat16), preferred_element_type=jnp.float32)
    rank = earlier.astype(jnp.int32)
    odd = (expert_range % 2 == 1)[None, :]
    rank = jnp.where(odd, CAP - 1 - rank, rank)
    slot_hit = member[:, :, None] & (rank[:, :, None] == jnp.arange(CAP, dtype=jnp.int32)[None, None, :])
    gather_rows = slot_hit.reshape(row_count, experts * CAP).astype(jnp.bfloat16)
    prob_of = jnp.sum(jnp.where(chosen, gate_probs[:, :, None], 0.0), axis=1)
    slot_prob = jnp.sum(jnp.where(slot_hit, prob_of[:, :, None], 0.0), axis=0).reshape(experts * CAP)
    send_x = jnp.dot(gather_rows.T, tokens, preferred_element_type=jnp.float32).astype(jnp.bfloat16)
    send_c = jnp.dot(gather_rows.T, cotangent, preferred_element_type=jnp.float32)
    send_grad = (slot_prob[:, None] * send_c).astype(jnp.bfloat16)
    lanes = per_device * CAP
    send_x = send_x.reshape(groups, lanes, model_width)
    send_grad = send_grad.reshape(groups, lanes, model_width)
    recv_x = lax.all_to_all(send_x, "expert", split_axis=0, concat_axis=0, tiled=True)
    recv_grad = lax.all_to_all(send_grad, "expert", split_axis=0, concat_axis=0, tiled=True)
    window = CAP + 4
    shift = lanes - window
    place = jnp.arange(window, dtype=jnp.int32)[None, :, None]
    outs, backs, firsts, seconds = [], [], [], []
    for local in range(per_device):
        low = local * shift
        rows_x = recv_x[:, low:low + window].reshape(groups * window, model_width)
        own = (place < CAP) if local == 0 else (place >= window - CAP)
        rows_grad = jnp.where(own, recv_grad[:, low:low + window], jnp.zeros((), jnp.bfloat16))
        rows_grad = rows_grad.reshape(groups * window, model_width)
        first_weight = weight_in[local]
        second_weight = weight_down[local]
        projected = jnp.dot(rows_x, first_weight, preferred_element_type=jnp.float32)
        pre_gate = projected[:, :FF]
        up_part = projected[:, FF:]
        sigmoid_gate = jax.nn.sigmoid(pre_gate)
        activated = pre_gate * sigmoid_gate
        hidden = (activated * up_part).astype(jnp.bfloat16)
        expert_out = jnp.dot(hidden, second_weight, preferred_element_type=jnp.float32).astype(
            jnp.bfloat16
        )
        hidden_grad = jnp.dot(rows_grad, second_weight.T, preferred_element_type=jnp.float32)
        gate_grad = hidden_grad * up_part * sigmoid_gate * (1.0 + pre_gate * (1.0 - sigmoid_gate))
        proj_grad = jnp.concatenate([gate_grad, hidden_grad * activated], axis=-1).astype(
            jnp.bfloat16
        )
        row_grad = jnp.dot(proj_grad, first_weight.T, preferred_element_type=jnp.float32).astype(
            jnp.bfloat16
        )
        outs.append(expert_out.reshape(groups, window, model_width))
        backs.append(row_grad.reshape(groups, window, model_width))
        firsts.append(jnp.dot(rows_x.T, proj_grad, preferred_element_type=jnp.float32))
        seconds.append(jnp.dot(hidden.T, rows_grad, preferred_element_type=jnp.float32))

    def merged(pieces):
        tile = window - shift
        seam = jnp.arange(tile, dtype=jnp.int32)[None, :, None] < CAP - shift
        middle = jnp.where(seam, pieces[0][:, shift:], pieces[1][:, :tile])
        return jnp.concatenate([pieces[0][:, :shift], middle, pieces[1][:, tile:]], axis=1)

    home_out = lax.all_to_all(merged(outs), "expert", split_axis=0, concat_axis=0, tiled=True)
    home_grad = lax.all_to_all(merged(backs), "expert", split_axis=0, concat_axis=0, tiled=True)
    grad_first = jnp.stack(firsts)
    grad_second = jnp.stack(seconds)
    reduced_in = lax.psum_scatter(
        grad_first.astype(jnp.bfloat16), "dp", scatter_dimension=1, tiled=True
    )
    reduced_down = lax.psum_scatter(
        grad_second.astype(jnp.bfloat16), "dp", scatter_dimension=2, tiled=True
    )
    partner_in, partner_down = swapped((reduced_in, reduced_down), "expert", 1)
    held_in = jnp.where(my_flag == 1, partner_in, reduced_in).astype(jnp.float32)
    held_down = jnp.where(my_flag == 1, partner_down, reduced_down).astype(jnp.float32)
    out_rows = home_out.reshape(experts * CAP, model_width)
    back_rows = home_grad.reshape(experts * CAP, model_width)
    combine = jnp.where(slot_hit, prob_of[:, :, None], 0.0).reshape(row_count, experts * CAP)
    layer_out = jnp.dot(
        combine, out_rows.astype(jnp.float32), precision=lax.Precision.HIGHEST,
        preferred_element_type=jnp.float32,
    ).astype(jnp.bfloat16)
    scores = jnp.dot(cotangent, out_rows.T, preferred_element_type=jnp.float32)
    rank_of = jnp.sum(jnp.where(chosen, rank[:, None, :], 0), axis=2)
    slot_of = expert_ids * CAP + rank_of
    gate_grads = jnp.take_along_axis(scores, slot_of, axis=1)
    token_grads = jnp.dot(gather_rows, back_rows, preferred_element_type=jnp.float32).astype(
        jnp.bfloat16
    )
    return (layer_out, gate_grads, token_grads, held_in, held_down)


def solution(mesh):
    in_specs = (
        P(("expert", "dp"), None),
        P(("expert", "dp"), None),
        P(("expert", "dp"), None),
        P(("expert", "dp"), None),
        P("expert", None, None),
        P("expert", None, None),
        P(),
    )
    out_specs = (
        P(("expert", "dp"), None),
        P(("expert", "dp"), None),
        P(("expert", "dp"), None),
        P("expert", "dp", None),
        P("expert", None, "dp"),
    )
    return jax.shard_map(body, mesh=mesh, in_specs=in_specs, out_specs=out_specs, check_vma=False)
```

```python
import jax
import jax.numpy as jnp
from jax import lax
from jax.sharding import PartitionSpec as P

FF = 384
TOP = 8
CAP = 20


def swapped(block, axis, apart):
    count = lax.axis_size(axis)
    route = []
    for low in range(count):
        high = low | 1 << apart
        if high != low and high < count:
            route += [(low, high), (high, low)]
    return lax.ppermute(block, axis, route)


def body(tokens, expert_ids, gate_probs, cotangent, weight_in, weight_down, swap_flag):
    row_count = tokens.shape[0]
    model_width = tokens.shape[1]
    per_device = weight_in.shape[0]
    groups = lax.axis_size("expert")
    experts = groups * per_device
    device_ids = jnp.arange(groups, dtype=jnp.int32)
    my_index = lax.axis_index("expert")
    my_flag = jnp.sum(jnp.where(device_ids == my_index, swap_flag, 0))
    expert_range = jnp.arange(experts, dtype=jnp.int32)
    chosen = expert_ids[:, :, None] == expert_range[None, None, :]
    member = jnp.any(chosen, axis=1)
    row_range = jnp.arange(row_count, dtype=jnp.int32)
    lower = (row_range[:, None] > row_range[None, :]).astype(jnp.bfloat16)
    earlier = jnp.dot(lower, member.astype(jnp.bfloat16), preferred_element_type=jnp.float32)
    rank = earlier.astype(jnp.int32)
    odd = (expert_range % 2 == 1)[None, :]
    rank = jnp.where(odd, CAP - 1 - rank, rank)
    slot_hit = member[:, :, None] & (rank[:, :, None] == jnp.arange(CAP, dtype=jnp.int32)[None, None, :])
    gather_rows = slot_hit.reshape(row_count, experts * CAP).astype(jnp.bfloat16)
    prob_of = jnp.sum(jnp.where(chosen, gate_probs[:, :, None], 0.0), axis=1)
    slot_prob = jnp.sum(jnp.where(slot_hit, prob_of[:, :, None], 0.0), axis=0).reshape(experts * CAP)
    send_x = jnp.dot(gather_rows.T, tokens, preferred_element_type=jnp.float32).astype(jnp.bfloat16)
    send_c = jnp.dot(gather_rows.T, cotangent, preferred_element_type=jnp.float32)
    send_grad = (slot_prob[:, None] * send_c).astype(jnp.bfloat16)
    lanes = per_device * CAP
    send_x = send_x.reshape(groups, lanes, model_width)
    send_grad = send_grad.reshape(groups, lanes, model_width)
    recv_x = lax.all_to_all(send_x, "expert", split_axis=0, concat_axis=0, tiled=True)
    recv_grad = lax.all_to_all(send_grad, "expert", split_axis=0, concat_axis=0, tiled=True)
    window = CAP + 4
    shift = lanes - window
    place = jnp.arange(window, dtype=jnp.int32)[None, :, None]
    forwards = []
    for local in range(per_device):
        low = local * shift
        rows_x = recv_x[:, low:low + window].reshape(groups * window, model_width)
        projected = jnp.dot(rows_x, weight_in[local], preferred_element_type=jnp.float32)
        pre_gate = projected[:, :FF]
        up_part = projected[:, FF:]
        sigmoid_gate = jax.nn.sigmoid(pre_gate)
        activated = pre_gate * sigmoid_gate
        hidden = (activated * up_part).astype(jnp.bfloat16)
        expert_out = jnp.dot(hidden, weight_down[local], preferred_element_type=jnp.float32).astype(
            jnp.bfloat16
        )
        forwards.append((rows_x, pre_gate, up_part, sigmoid_gate, activated, hidden, expert_out))

    def merged(pieces):
        tile = window - shift
        seam = jnp.arange(tile, dtype=jnp.int32)[None, :, None] < CAP - shift
        middle = jnp.where(seam, pieces[0][:, shift:], pieces[1][:, :tile])
        return jnp.concatenate([pieces[0][:, :shift], middle, pieces[1][:, tile:]], axis=1)

    send_out = merged([f[-1].reshape(groups, window, model_width) for f in forwards])
    send_out, recv_grad = lax.optimization_barrier((send_out, recv_grad))
    home_out = lax.all_to_all(send_out, "expert", split_axis=0, concat_axis=0, tiled=True)
    backs, firsts, seconds = [], [], []
    for local in range(per_device):
        low = local * shift
        rows_x, pre_gate, up_part, sigmoid_gate, activated, hidden, _ = forwards[local]
        own = (place < CAP) if local == 0 else (place >= window - CAP)
        rows_grad = jnp.where(own, recv_grad[:, low:low + window], jnp.zeros((), jnp.bfloat16))
        rows_grad = rows_grad.reshape(groups * window, model_width)
        hidden_grad = jnp.dot(rows_grad, weight_down[local].T, preferred_element_type=jnp.float32)
        gate_grad = hidden_grad * up_part * sigmoid_gate * (1.0 + pre_gate * (1.0 - sigmoid_gate))
        proj_grad = jnp.concatenate([gate_grad, hidden_grad * activated], axis=-1).astype(
            jnp.bfloat16
        )
        row_grad = jnp.dot(proj_grad, weight_in[local].T, preferred_element_type=jnp.float32).astype(
            jnp.bfloat16
        )
        backs.append(row_grad.reshape(groups, window, model_width))
        firsts.append(jnp.dot(rows_x.T, proj_grad, preferred_element_type=jnp.float32))
        seconds.append(jnp.dot(hidden.T, rows_grad, preferred_element_type=jnp.float32))
    grad_first = jnp.stack(firsts)
    grad_second = jnp.stack(seconds)
    reduced_in = lax.psum_scatter(
        grad_first.astype(jnp.bfloat16), "dp", scatter_dimension=1, tiled=True
    )
    reduced_down = lax.psum_scatter(
        grad_second.astype(jnp.bfloat16), "dp", scatter_dimension=2, tiled=True
    )
    send_back, reduced_in = lax.optimization_barrier((merged(backs), reduced_in))
    home_grad = lax.all_to_all(send_back, "expert", split_axis=0, concat_axis=0, tiled=True)
    partner_in, partner_down = swapped((reduced_in, reduced_down), "expert", 1)
    held_in = jnp.where(my_flag == 1, partner_in, reduced_in).astype(jnp.float32)
    held_down = jnp.where(my_flag == 1, partner_down, reduced_down).astype(jnp.float32)
    out_rows = home_out.reshape(experts * CAP, model_width)
    back_rows = home_grad.reshape(experts * CAP, model_width)
    combine = jnp.where(slot_hit, prob_of[:, :, None], 0.0).reshape(row_count, experts * CAP)
    layer_out = jnp.dot(
        combine, out_rows.astype(jnp.float32), precision=lax.Precision.HIGHEST,
        preferred_element_type=jnp.float32,
    ).astype(jnp.bfloat16)
    scores = jnp.dot(cotangent, out_rows.T, preferred_element_type=jnp.float32)
    rank_of = jnp.sum(jnp.where(chosen, rank[:, None, :], 0), axis=2)
    slot_of = expert_ids * CAP + rank_of
    gate_grads = jnp.take_along_axis(scores, slot_of, axis=1)
    token_grads = jnp.dot(gather_rows, back_rows, preferred_element_type=jnp.float32).astype(
        jnp.bfloat16
    )
    return (layer_out, gate_grads, token_grads, held_in, held_down)


def solution(mesh):
    in_specs = (
        P(("expert", "dp"), None),
        P(("expert", "dp"), None),
        P(("expert", "dp"), None),
        P(("expert", "dp"), None),
        P("expert", None, None),
        P("expert", None, None),
        P(),
    )
    out_specs = (
        P(("expert", "dp"), None),
        P(("expert", "dp"), None),
        P(("expert", "dp"), None),
        P("expert", "dp", None),
        P("expert", None, "dp"),
    )
    return jax.shard_map(body, mesh=mesh, in_specs=in_specs, out_specs=out_specs, check_vma=False)
```

```python
import jax
import jax.numpy as jnp
from jax import lax
from jax.sharding import PartitionSpec as P

FF = 384
TOP = 8
CAP = 20


def swapped(block, axis, apart):
    count = lax.axis_size(axis)
    route = []
    for low in range(count):
        high = low | 1 << apart
        if high != low and high < count:
            route += [(low, high), (high, low)]
    return lax.ppermute(block, axis, route)


def body(tokens, expert_ids, gate_probs, cotangent, weight_in, weight_down, swap_flag):
    row_count = tokens.shape[0]
    model_width = tokens.shape[1]
    per_device = weight_in.shape[0]
    groups = lax.axis_size("expert")
    experts = groups * per_device
    device_ids = jnp.arange(groups, dtype=jnp.int32)
    my_index = lax.axis_index("expert")
    my_flag = jnp.sum(jnp.where(device_ids == my_index, swap_flag, 0))
    expert_range = jnp.arange(experts, dtype=jnp.int32)
    chosen = expert_ids[:, :, None] == expert_range[None, None, :]
    member = jnp.any(chosen, axis=1)
    row_range = jnp.arange(row_count, dtype=jnp.int32)
    lower = (row_range[:, None] > row_range[None, :]).astype(jnp.bfloat16)
    earlier = jnp.dot(lower, member.astype(jnp.bfloat16), preferred_element_type=jnp.float32)
    rank = earlier.astype(jnp.int32)
    odd = (expert_range % 2 == 1)[None, :]
    rank = jnp.where(odd, CAP - 1 - rank, rank)
    slot_hit = member[:, :, None] & (rank[:, :, None] == jnp.arange(CAP, dtype=jnp.int32)[None, None, :])
    gather_rows = slot_hit.reshape(row_count, experts * CAP).astype(jnp.bfloat16)
    prob_of = jnp.sum(jnp.where(chosen, gate_probs[:, :, None], 0.0), axis=1)
    slot_prob = jnp.sum(jnp.where(slot_hit, prob_of[:, :, None], 0.0), axis=0).reshape(experts * CAP)
    send_x = jnp.dot(gather_rows.T, tokens, preferred_element_type=jnp.float32).astype(jnp.bfloat16)
    send_c = jnp.dot(gather_rows.T, cotangent, preferred_element_type=jnp.float32)
    send_grad = (slot_prob[:, None] * send_c).astype(jnp.bfloat16)
    lanes = per_device * CAP
    send_x = send_x.reshape(groups, lanes, model_width)
    send_grad = send_grad.reshape(groups, lanes, model_width)
    recv_x = lax.all_to_all(send_x, "expert", split_axis=0, concat_axis=0, tiled=True)
    recv_grad = lax.all_to_all(send_grad, "expert", split_axis=0, concat_axis=0, tiled=True)
    window = CAP + 4
    shift = lanes - window
    place = jnp.arange(window, dtype=jnp.int32)[None, :, None]
    forwards = []
    for local in range(per_device):
        low = local * shift
        rows_x = recv_x[:, low:low + window]
        projected = jnp.einsum("ncd,df->ncf", rows_x, weight_in[local], preferred_element_type=jnp.float32)
        pre_gate = projected[..., :FF]
        up_part = projected[..., FF:]
        sigmoid_gate = jax.nn.sigmoid(pre_gate)
        activated = pre_gate * sigmoid_gate
        own = (place < CAP) if local == 0 else (place >= window - CAP)
        hidden = jnp.where(own, activated * up_part, 0.0).astype(jnp.bfloat16)
        expert_out = jnp.einsum(
            "ncf,fd->ncd", hidden, weight_down[local], preferred_element_type=jnp.float32
        ).astype(jnp.bfloat16)
        forwards.append((rows_x, pre_gate, up_part, sigmoid_gate, activated, hidden, own, expert_out))

    def merged(pieces):
        tile = window - shift
        seam = jnp.arange(tile, dtype=jnp.int32)[None, :, None] < CAP - shift
        middle = jnp.where(seam, pieces[0][:, shift:], pieces[1][:, :tile])
        return jnp.concatenate([pieces[0][:, :shift], middle, pieces[1][:, tile:]], axis=1)

    send_out = merged([f[-1] for f in forwards])
    send_out, recv_grad = lax.optimization_barrier((send_out, recv_grad))
    home_out = lax.all_to_all(send_out, "expert", split_axis=0, concat_axis=0, tiled=True)
    backs, firsts, seconds = [], [], []
    for local in range(per_device):
        low = local * shift
        rows_x, pre_gate, up_part, sigmoid_gate, activated, hidden, own, _ = forwards[local]
        rows_grad = recv_grad[:, low:low + window]
        hidden_grad = jnp.einsum(
            "ncd,fd->ncf", rows_grad, weight_down[local], preferred_element_type=jnp.float32
        )
        hidden_grad = jnp.where(own, hidden_grad, 0.0)
        gate_grad = hidden_grad * up_part * sigmoid_gate * (1.0 + pre_gate * (1.0 - sigmoid_gate))
        proj_grad = jnp.concatenate([gate_grad, hidden_grad * activated], axis=-1).astype(
            jnp.bfloat16
        )
        row_grad = jnp.einsum(
            "ncf,df->ncd", proj_grad, weight_in[local], preferred_element_type=jnp.float32
        ).astype(jnp.bfloat16)
        backs.append(row_grad)
        firsts.append(jnp.einsum("ncd,ncf->df", rows_x, proj_grad, preferred_element_type=jnp.float32))
        seconds.append(jnp.einsum("ncf,ncd->fd", hidden, rows_grad, preferred_element_type=jnp.float32))
    grad_first = jnp.stack(firsts)
    grad_second = jnp.stack(seconds)
    reduced_in = lax.psum_scatter(
        grad_first.astype(jnp.bfloat16), "dp", scatter_dimension=1, tiled=True
    )
    reduced_down = lax.psum_scatter(
        grad_second.astype(jnp.bfloat16), "dp", scatter_dimension=2, tiled=True
    )
    send_back, reduced_in = lax.optimization_barrier((merged(backs), reduced_in))
    home_grad = lax.all_to_all(send_back, "expert", split_axis=0, concat_axis=0, tiled=True)
    partner_in, partner_down = swapped((reduced_in, reduced_down), "expert", 1)
    held_in = jnp.where(my_flag == 1, partner_in, reduced_in).astype(jnp.float32)
    held_down = jnp.where(my_flag == 1, partner_down, reduced_down).astype(jnp.float32)
    out_rows = home_out.reshape(experts * CAP, model_width)
    back_rows = home_grad.reshape(experts * CAP, model_width)
    combine = jnp.where(slot_hit, prob_of[:, :, None], 0.0).reshape(row_count, experts * CAP)
    layer_out = jnp.dot(
        combine, out_rows.astype(jnp.float32), precision=lax.Precision.HIGHEST,
        preferred_element_type=jnp.float32,
    ).astype(jnp.bfloat16)
    scores = jnp.dot(cotangent, out_rows.T, preferred_element_type=jnp.float32)
    rank_of = jnp.sum(jnp.where(chosen, rank[:, None, :], 0), axis=2)
    slot_of = expert_ids * CAP + rank_of
    gate_grads = jnp.take_along_axis(scores, slot_of, axis=1)
    token_grads = jnp.dot(gather_rows, back_rows, preferred_element_type=jnp.float32).astype(
        jnp.bfloat16
    )
    return (layer_out, gate_grads, token_grads, held_in, held_down)


def solution(mesh):
    in_specs = (
        P(("expert", "dp"), None),
        P(("expert", "dp"), None),
        P(("expert", "dp"), None),
        P(("expert", "dp"), None),
        P("expert", None, None),
        P("expert", None, None),
        P(),
    )
    out_specs = (
        P(("expert", "dp"), None),
        P(("expert", "dp"), None),
        P(("expert", "dp"), None),
        P("expert", "dp", None),
        P("expert", None, "dp"),
    )
    return jax.shard_map(body, mesh=mesh, in_specs=in_specs, out_specs=out_specs, check_vma=False)
```

```python
import jax
import jax.numpy as jnp
from jax import lax
from jax.sharding import PartitionSpec as P

FF = 384
TOP = 8
CAP = 20


def swapped(block, axis, apart):
    count = lax.axis_size(axis)
    route = []
    for low in range(count):
        high = low | 1 << apart
        if high != low and high < count:
            route += [(low, high), (high, low)]
    return lax.ppermute(block, axis, route)


def body(tokens, expert_ids, gate_probs, cotangent, weight_in, weight_down, swap_flag):
    row_count = tokens.shape[0]
    model_width = tokens.shape[1]
    per_device = weight_in.shape[0]
    groups = lax.axis_size("expert")
    experts = groups * per_device
    device_ids = jnp.arange(groups, dtype=jnp.int32)
    my_index = lax.axis_index("expert")
    my_flag = jnp.sum(jnp.where(device_ids == my_index, swap_flag, 0))
    expert_range = jnp.arange(experts, dtype=jnp.int32)
    chosen = expert_ids[:, :, None] == expert_range[None, None, :]
    member = jnp.any(chosen, axis=1)
    row_range = jnp.arange(row_count, dtype=jnp.int32)
    lower = (row_range[:, None] > row_range[None, :]).astype(jnp.bfloat16)
    earlier = jnp.dot(lower, member.astype(jnp.bfloat16), preferred_element_type=jnp.float32)
    rank = earlier.astype(jnp.int32)
    odd = (expert_range % 2 == 1)[None, :]
    rank = jnp.where(odd, CAP - 1 - rank, rank)
    slot_hit = member[:, :, None] & (rank[:, :, None] == jnp.arange(CAP, dtype=jnp.int32)[None, None, :])
    gather_rows = slot_hit.reshape(row_count, experts * CAP).astype(jnp.bfloat16)
    prob_of = jnp.sum(jnp.where(chosen, gate_probs[:, :, None], 0.0), axis=1)
    slot_prob = jnp.sum(jnp.where(slot_hit, prob_of[:, :, None], 0.0), axis=0).reshape(experts * CAP)
    send_x = jnp.dot(gather_rows.T, tokens, preferred_element_type=jnp.float32).astype(jnp.bfloat16)
    send_c = jnp.dot(gather_rows.T, cotangent, preferred_element_type=jnp.float32)
    send_grad = (slot_prob[:, None] * send_c).astype(jnp.bfloat16)
    lanes = per_device * CAP
    send_x = send_x.reshape(groups, lanes, model_width)
    send_grad = send_grad.reshape(groups, lanes, model_width)
    recv_both = lax.all_to_all(
        jnp.concatenate([send_x, send_grad], axis=1), "expert", split_axis=0, concat_axis=0, tiled=True
    )
    recv_x = recv_both[:, :lanes]
    recv_grad = recv_both[:, lanes:]
    window = CAP + 4
    shift = lanes - window
    place = jnp.arange(window, dtype=jnp.int32)[None, :, None]
    forwards = []
    for local in range(per_device):
        low = local * shift
        rows_x = recv_x[:, low:low + window].reshape(groups * window, model_width)
        projected = jnp.dot(rows_x, weight_in[local], preferred_element_type=jnp.float32)
        pre_gate = projected[:, :FF]
        up_part = projected[:, FF:]
        sigmoid_gate = jax.nn.sigmoid(pre_gate)
        activated = pre_gate * sigmoid_gate
        hidden = (activated * up_part).astype(jnp.bfloat16)
        expert_out = jnp.dot(hidden, weight_down[local], preferred_element_type=jnp.float32).astype(
            jnp.bfloat16
        )
        forwards.append((rows_x, pre_gate, up_part, sigmoid_gate, activated, hidden, expert_out))

    def merged(pieces):
        tile = window - shift
        seam = jnp.arange(tile, dtype=jnp.int32)[None, :, None] < CAP - shift
        middle = jnp.where(seam, pieces[0][:, shift:], pieces[1][:, :tile])
        return jnp.concatenate([pieces[0][:, :shift], middle, pieces[1][:, tile:]], axis=1)

    send_out = merged([f[-1].reshape(groups, window, model_width) for f in forwards])
    send_out, recv_grad = lax.optimization_barrier((send_out, recv_grad))
    home_out = lax.all_to_all(send_out, "expert", split_axis=0, concat_axis=0, tiled=True)
    backs, firsts, seconds = [], [], []
    for local in range(per_device):
        low = local * shift
        rows_x, pre_gate, up_part, sigmoid_gate, activated, hidden, _ = forwards[local]
        own = (place < CAP) if local == 0 else (place >= window - CAP)
        rows_grad = jnp.where(own, recv_grad[:, low:low + window], jnp.zeros((), jnp.bfloat16))
        rows_grad = rows_grad.reshape(groups * window, model_width)
        hidden_grad = jnp.dot(rows_grad, weight_down[local].T, preferred_element_type=jnp.float32)
        gate_grad = hidden_grad * up_part * sigmoid_gate * (1.0 + pre_gate * (1.0 - sigmoid_gate))
        proj_grad = jnp.concatenate([gate_grad, hidden_grad * activated], axis=-1).astype(
            jnp.bfloat16
        )
        row_grad = jnp.dot(proj_grad, weight_in[local].T, preferred_element_type=jnp.float32).astype(
            jnp.bfloat16
        )
        backs.append(row_grad.reshape(groups, window, model_width))
        firsts.append(jnp.dot(rows_x.T, proj_grad, preferred_element_type=jnp.float32))
        seconds.append(jnp.dot(hidden.T, rows_grad, preferred_element_type=jnp.float32))
    grad_first = jnp.stack(firsts)
    grad_second = jnp.stack(seconds)
    reduced_in = lax.psum_scatter(
        grad_first.astype(jnp.bfloat16), "dp", scatter_dimension=1, tiled=True
    )
    reduced_down = lax.psum_scatter(
        grad_second.astype(jnp.bfloat16), "dp", scatter_dimension=2, tiled=True
    )
    send_back, reduced_in = lax.optimization_barrier((merged(backs), reduced_in))
    home_grad = lax.all_to_all(send_back, "expert", split_axis=0, concat_axis=0, tiled=True)
    partner_in, partner_down = swapped((reduced_in, reduced_down), "expert", 1)
    held_in = jnp.where(my_flag == 1, partner_in, reduced_in).astype(jnp.float32)
    held_down = jnp.where(my_flag == 1, partner_down, reduced_down).astype(jnp.float32)
    out_rows = home_out.reshape(experts * CAP, model_width)
    back_rows = home_grad.reshape(experts * CAP, model_width)
    combine = jnp.where(slot_hit, prob_of[:, :, None], 0.0).reshape(row_count, experts * CAP)
    layer_out = jnp.dot(
        combine, out_rows.astype(jnp.float32), precision=lax.Precision.HIGHEST,
        preferred_element_type=jnp.float32,
    ).astype(jnp.bfloat16)
    scores = jnp.dot(cotangent, out_rows.T, preferred_element_type=jnp.float32)
    rank_of = jnp.sum(jnp.where(chosen, rank[:, None, :], 0), axis=2)
    slot_of = expert_ids * CAP + rank_of
    gate_grads = jnp.take_along_axis(scores, slot_of, axis=1)
    token_grads = jnp.dot(gather_rows, back_rows, preferred_element_type=jnp.float32).astype(
        jnp.bfloat16
    )
    return (layer_out, gate_grads, token_grads, held_in, held_down)


def solution(mesh):
    in_specs = (
        P(("expert", "dp"), None),
        P(("expert", "dp"), None),
        P(("expert", "dp"), None),
        P(("expert", "dp"), None),
        P("expert", None, None),
        P("expert", None, None),
        P(),
    )
    out_specs = (
        P(("expert", "dp"), None),
        P(("expert", "dp"), None),
        P(("expert", "dp"), None),
        P("expert", "dp", None),
        P("expert", None, "dp"),
    )
    return jax.shard_map(body, mesh=mesh, in_specs=in_specs, out_specs=out_specs, check_vma=False)
```

```python
import jax
import jax.numpy as jnp
from jax import lax
from jax.sharding import PartitionSpec as P

FF = 384
TOP = 8
CAP = 20


def swapped(block, axis, apart):
    count = lax.axis_size(axis)
    route = []
    for low in range(count):
        high = low | 1 << apart
        if high != low and high < count:
            route += [(low, high), (high, low)]
    return lax.ppermute(block, axis, route)


def body(tokens, expert_ids, gate_probs, cotangent, weight_in, weight_down, swap_flag):
    row_count = tokens.shape[0]
    model_width = tokens.shape[1]
    per_device = weight_in.shape[0]
    groups = lax.axis_size("expert")
    experts = groups * per_device
    device_ids = jnp.arange(groups, dtype=jnp.int32)
    my_index = lax.axis_index("expert")
    my_flag = jnp.sum(jnp.where(device_ids == my_index, swap_flag, 0))
    expert_range = jnp.arange(experts, dtype=jnp.int32)
    chosen = expert_ids[:, :, None] == expert_range[None, None, :]
    member = jnp.any(chosen, axis=1)
    row_range = jnp.arange(row_count, dtype=jnp.int32)
    lower = (row_range[:, None] > row_range[None, :]).astype(jnp.bfloat16)
    earlier = jnp.dot(lower, member.astype(jnp.bfloat16), preferred_element_type=jnp.float32)
    rank = earlier.astype(jnp.int32)
    odd = (expert_range % 2 == 1)[None, :]
    rank = jnp.where(odd, CAP - 1 - rank, rank)
    slot_hit = member[:, :, None] & (rank[:, :, None] == jnp.arange(CAP, dtype=jnp.int32)[None, None, :])
    gather_rows = slot_hit.reshape(row_count, experts * CAP).astype(jnp.bfloat16)
    prob_of = jnp.sum(jnp.where(chosen, gate_probs[:, :, None], 0.0), axis=1)
    slot_prob = jnp.sum(jnp.where(slot_hit, prob_of[:, :, None], 0.0), axis=0).reshape(experts * CAP)
    send_x = jnp.dot(gather_rows.T, tokens, preferred_element_type=jnp.float32).astype(jnp.bfloat16)
    send_c = jnp.dot(gather_rows.T, cotangent, preferred_element_type=jnp.float32)
    send_grad = (slot_prob[:, None] * send_c).astype(jnp.bfloat16)
    lanes = per_device * CAP
    send_x = send_x.reshape(groups, lanes, model_width)
    send_grad = send_grad.reshape(groups, lanes, model_width)
    recv_x = lax.all_to_all(send_x, "expert", split_axis=0, concat_axis=0, tiled=True)
    recv_grad = lax.all_to_all(send_grad, "expert", split_axis=0, concat_axis=0, tiled=True)
    window = CAP + 4
    shift = lanes - window
    place = jnp.arange(window, dtype=jnp.int32)[None, :, None]
    forwards = []
    for local in range(per_device):
        low = local * shift
        rows_x = recv_x[:, low:low + window].reshape(groups * window, model_width)
        projected = jnp.dot(rows_x, weight_in[local], preferred_element_type=jnp.float32)
        pre_gate = projected[:, :FF]
        up_part = projected[:, FF:]
        sigmoid_gate = jax.nn.sigmoid(pre_gate)
        activated = pre_gate * sigmoid_gate
        hidden = (activated * up_part).astype(jnp.bfloat16)
        expert_out = jnp.dot(hidden, weight_down[local], preferred_element_type=jnp.float32).astype(
            jnp.bfloat16
        )
        forwards.append((rows_x, pre_gate, up_part, sigmoid_gate, activated, hidden, expert_out))

    def merged(pieces):
        tile = window - shift
        seam = jnp.arange(tile, dtype=jnp.int32)[None, :, None] < CAP - shift
        middle = jnp.where(seam, pieces[0][:, shift:], pieces[1][:, :tile])
        return jnp.concatenate([pieces[0][:, :shift], middle, pieces[1][:, tile:]], axis=1)

    send_out = merged([f[-1].reshape(groups, window, model_width) for f in forwards])
    send_out, recv_grad = lax.optimization_barrier((send_out, recv_grad))
    home_out = lax.all_to_all(send_out, "expert", split_axis=0, concat_axis=0, tiled=True)
    windows, seconds = [], []
    for local in range(per_device):
        low = local * shift
        hidden = forwards[local][5]
        own = (place < CAP) if local == 0 else (place >= window - CAP)
        rows_grad = jnp.where(own, recv_grad[:, low:low + window], jnp.zeros((), jnp.bfloat16))
        rows_grad = rows_grad.reshape(groups * window, model_width)
        windows.append(rows_grad)
        seconds.append(jnp.dot(hidden.T, rows_grad, preferred_element_type=jnp.float32))
    grad_second = jnp.stack(seconds)
    windows, grad_second = lax.optimization_barrier((windows, grad_second))
    reduced_down = lax.psum_scatter(
        grad_second.astype(jnp.bfloat16), "dp", scatter_dimension=2, tiled=True
    )
    backs, firsts = [], []
    for local in range(per_device):
        rows_x, pre_gate, up_part, sigmoid_gate, activated, hidden, _ = forwards[local]
        rows_grad = windows[local]
        hidden_grad = jnp.dot(rows_grad, weight_down[local].T, preferred_element_type=jnp.float32)
        gate_grad = hidden_grad * up_part * sigmoid_gate * (1.0 + pre_gate * (1.0 - sigmoid_gate))
        proj_grad = jnp.concatenate([gate_grad, hidden_grad * activated], axis=-1).astype(
            jnp.bfloat16
        )
        row_grad = jnp.dot(proj_grad, weight_in[local].T, preferred_element_type=jnp.float32).astype(
            jnp.bfloat16
        )
        backs.append(row_grad.reshape(groups, window, model_width))
        firsts.append((rows_x, proj_grad))
    send_back, firsts, reduced_down = lax.optimization_barrier((merged(backs), firsts, reduced_down))
    firsts = [jnp.dot(a.T, b, preferred_element_type=jnp.float32) for a, b in firsts]
    grad_first, home_out = lax.optimization_barrier((jnp.stack(firsts), home_out))
    reduced_in = lax.psum_scatter(
        grad_first.astype(jnp.bfloat16), "dp", scatter_dimension=1, tiled=True
    )
    home_grad = lax.all_to_all(send_back, "expert", split_axis=0, concat_axis=0, tiled=True)
    partner_in, partner_down = swapped((reduced_in, reduced_down), "expert", 1)
    held_in = jnp.where(my_flag == 1, partner_in, reduced_in).astype(jnp.float32)
    held_down = jnp.where(my_flag == 1, partner_down, reduced_down).astype(jnp.float32)
    out_rows = home_out.reshape(experts * CAP, model_width)
    back_rows = home_grad.reshape(experts * CAP, model_width)
    combine = jnp.where(slot_hit, prob_of[:, :, None], 0.0).reshape(row_count, experts * CAP)
    layer_out = jnp.dot(
        combine, out_rows.astype(jnp.float32), precision=lax.Precision.HIGHEST,
        preferred_element_type=jnp.float32,
    ).astype(jnp.bfloat16)
    scores = jnp.dot(cotangent, out_rows.T, preferred_element_type=jnp.float32)
    rank_of = jnp.sum(jnp.where(chosen, rank[:, None, :], 0), axis=2)
    slot_of = expert_ids * CAP + rank_of
    gate_grads = jnp.take_along_axis(scores, slot_of, axis=1)
    token_grads = jnp.dot(gather_rows, back_rows, preferred_element_type=jnp.float32).astype(
        jnp.bfloat16
    )
    return (layer_out, gate_grads, token_grads, held_in, held_down)


def solution(mesh):
    in_specs = (
        P(("expert", "dp"), None),
        P(("expert", "dp"), None),
        P(("expert", "dp"), None),
        P(("expert", "dp"), None),
        P("expert", None, None),
        P("expert", None, None),
        P(),
    )
    out_specs = (
        P(("expert", "dp"), None),
        P(("expert", "dp"), None),
        P(("expert", "dp"), None),
        P("expert", "dp", None),
        P("expert", None, "dp"),
    )
    return jax.shard_map(body, mesh=mesh, in_specs=in_specs, out_specs=out_specs, check_vma=False)
```

```python
import jax
import jax.numpy as jnp
from jax import lax
from jax.sharding import PartitionSpec as P

FF = 384
TOP = 8
CAP = 20


def swapped(block, axis, apart):
    count = lax.axis_size(axis)
    route = []
    for low in range(count):
        high = low | 1 << apart
        if high != low and high < count:
            route += [(low, high), (high, low)]
    return lax.ppermute(block, axis, route)


def body(tokens, expert_ids, gate_probs, cotangent, weight_in, weight_down, swap_flag):
    row_count = tokens.shape[0]
    model_width = tokens.shape[1]
    per_device = weight_in.shape[0]
    groups = lax.axis_size("expert")
    experts = groups * per_device
    device_ids = jnp.arange(groups, dtype=jnp.int32)
    my_index = lax.axis_index("expert")
    my_flag = jnp.sum(jnp.where(device_ids == my_index, swap_flag, 0))
    expert_range = jnp.arange(experts, dtype=jnp.int32)
    chosen = expert_ids[:, :, None] == expert_range[None, None, :]
    member = jnp.any(chosen, axis=1)
    row_range = jnp.arange(row_count, dtype=jnp.int32)
    lower = (row_range[:, None] > row_range[None, :]).astype(jnp.bfloat16)
    earlier = jnp.dot(lower, member.astype(jnp.bfloat16), preferred_element_type=jnp.float32)
    rank = earlier.astype(jnp.int32)
    odd = (expert_range % 2 == 1)[None, :]
    rank = jnp.where(odd, CAP - 1 - rank, rank)
    slot_hit = member[:, :, None] & (rank[:, :, None] == jnp.arange(CAP, dtype=jnp.int32)[None, None, :])
    gather_rows = slot_hit.reshape(row_count, experts * CAP).astype(jnp.bfloat16)
    prob_of = jnp.sum(jnp.where(chosen, gate_probs[:, :, None], 0.0), axis=1)
    slot_prob = jnp.sum(jnp.where(slot_hit, prob_of[:, :, None], 0.0), axis=0).reshape(experts * CAP)
    send_x = jnp.dot(gather_rows.T, tokens, preferred_element_type=jnp.float32).astype(jnp.bfloat16)
    send_c = jnp.dot(gather_rows.T, cotangent, preferred_element_type=jnp.float32)
    send_grad = (slot_prob[:, None] * send_c).astype(jnp.bfloat16)
    lanes = per_device * CAP
    send_x = send_x.reshape(groups, lanes, model_width)
    send_grad = send_grad.reshape(groups, lanes, model_width)
    recv_x = lax.all_to_all(send_x, "expert", split_axis=0, concat_axis=0, tiled=True)
    recv_grad = lax.all_to_all(send_grad, "expert", split_axis=0, concat_axis=0, tiled=True)
    window = CAP + 4
    shift = lanes - window
    place = jnp.arange(window, dtype=jnp.int32)[None, :, None]
    forwards = []
    for local in range(per_device):
        low = local * shift
        rows_x = recv_x[:, low:low + window].reshape(groups * window, model_width)
        projected = jnp.dot(rows_x, weight_in[local], preferred_element_type=jnp.float32)
        pre_gate = projected[:, :FF]
        up_part = projected[:, FF:]
        sigmoid_gate = jax.nn.sigmoid(pre_gate)
        activated = pre_gate * sigmoid_gate
        hidden = (activated * up_part).astype(jnp.bfloat16)
        expert_out = jnp.dot(hidden, weight_down[local], preferred_element_type=jnp.float32).astype(
            jnp.bfloat16
        )
        forwards.append((rows_x, pre_gate, up_part, sigmoid_gate, activated, hidden, expert_out))

    def merged(pieces):
        tile = window - shift
        seam = jnp.arange(tile, dtype=jnp.int32)[None, :, None] < CAP - shift
        middle = jnp.where(seam, pieces[0][:, shift:], pieces[1][:, :tile])
        return jnp.concatenate([pieces[0][:, :shift], middle, pieces[1][:, tile:]], axis=1)

    send_out = merged([f[-1].reshape(groups, window, model_width) for f in forwards])
    send_out, recv_grad = lax.optimization_barrier((send_out, recv_grad))
    home_out = lax.all_to_all(send_out, "expert", split_axis=0, concat_axis=0, tiled=True)
    whole_grad = recv_grad.reshape(groups * lanes, model_width)
    lane = jnp.arange(lanes, dtype=jnp.int32)[None, :, None]
    windows, seconds = [], []
    for local in range(per_device):
        low = local * shift
        hidden = forwards[local][5].reshape(groups, window, FF)
        own = (place < CAP) if local == 0 else (place >= window - CAP)
        padded = jnp.pad(hidden, ((0, 0), (low, lanes - window - low), (0, 0)))
        mine = (lane < CAP) if local == 0 else (lane >= CAP)
        padded = jnp.where(mine, padded, jnp.zeros((), jnp.bfloat16)).reshape(groups * lanes, FF)
        seconds.append(jnp.dot(padded.T, whole_grad, preferred_element_type=jnp.float32))
    recv_grad, seconds = lax.optimization_barrier((recv_grad, seconds))
    for local in range(per_device):
        low = local * shift
        own = (place < CAP) if local == 0 else (place >= window - CAP)
        rows_grad = jnp.where(own, recv_grad[:, low:low + window], jnp.zeros((), jnp.bfloat16))
        windows.append(rows_grad.reshape(groups * window, model_width))
    reduced_down = jnp.stack([
        lax.psum_scatter(part.astype(jnp.bfloat16), "dp", scatter_dimension=1, tiled=True)
        for part in seconds
    ])
    backs, firsts = [], []
    for local in range(per_device):
        rows_x, pre_gate, up_part, sigmoid_gate, activated, hidden, _ = forwards[local]
        rows_grad = windows[local]
        hidden_grad = jnp.dot(rows_grad, weight_down[local].T, preferred_element_type=jnp.float32)
        gate_grad = hidden_grad * up_part * sigmoid_gate * (1.0 + pre_gate * (1.0 - sigmoid_gate))
        proj_grad = jnp.concatenate([gate_grad, hidden_grad * activated], axis=-1).astype(
            jnp.bfloat16
        )
        row_grad = jnp.dot(proj_grad, weight_in[local].T, preferred_element_type=jnp.float32).astype(
            jnp.bfloat16
        )
        backs.append(row_grad.reshape(groups, window, model_width))
        firsts.append((rows_x, proj_grad))
    send_back, firsts, reduced_down = lax.optimization_barrier((merged(backs), firsts, reduced_down))
    firsts = [jnp.dot(a.T, b, preferred_element_type=jnp.float32) for a, b in firsts]
    grad_first, home_out = lax.optimization_barrier((jnp.stack(firsts), home_out))
    reduced_in = lax.psum_scatter(
        grad_first.astype(jnp.bfloat16), "dp", scatter_dimension=1, tiled=True
    )
    home_grad = lax.all_to_all(send_back, "expert", split_axis=0, concat_axis=0, tiled=True)
    partner_in, partner_down = swapped((reduced_in, reduced_down), "expert", 1)
    held_in = jnp.where(my_flag == 1, partner_in, reduced_in).astype(jnp.float32)
    held_down = jnp.where(my_flag == 1, partner_down, reduced_down).astype(jnp.float32)
    out_rows = home_out.reshape(experts * CAP, model_width)
    back_rows = home_grad.reshape(experts * CAP, model_width)
    combine = jnp.where(slot_hit, prob_of[:, :, None], 0.0).reshape(row_count, experts * CAP)
    layer_out = jnp.dot(
        combine, out_rows.astype(jnp.float32), precision=lax.Precision.HIGHEST,
        preferred_element_type=jnp.float32,
    ).astype(jnp.bfloat16)
    scores = jnp.dot(cotangent, out_rows.T, preferred_element_type=jnp.float32)
    rank_of = jnp.sum(jnp.where(chosen, rank[:, None, :], 0), axis=2)
    slot_of = expert_ids * CAP + rank_of
    gate_grads = jnp.take_along_axis(scores, slot_of, axis=1)
    token_grads = jnp.dot(gather_rows, back_rows, preferred_element_type=jnp.float32).astype(
        jnp.bfloat16
    )
    return (layer_out, gate_grads, token_grads, held_in, held_down)


def solution(mesh):
    in_specs = (
        P(("expert", "dp"), None),
        P(("expert", "dp"), None),
        P(("expert", "dp"), None),
        P(("expert", "dp"), None),
        P("expert", None, None),
        P("expert", None, None),
        P(),
    )
    out_specs = (
        P(("expert", "dp"), None),
        P(("expert", "dp"), None),
        P(("expert", "dp"), None),
        P("expert", "dp", None),
        P("expert", None, "dp"),
    )
    return jax.shard_map(body, mesh=mesh, in_specs=in_specs, out_specs=out_specs, check_vma=False)
```

```python
import jax
import jax.numpy as jnp
from jax import lax
from jax.sharding import PartitionSpec as P

FF = 384
TOP = 8
CAP = 20


def swapped(block, axis, apart):
    count = lax.axis_size(axis)
    route = []
    for low in range(count):
        high = low | 1 << apart
        if high != low and high < count:
            route += [(low, high), (high, low)]
    return lax.ppermute(block, axis, route)


def body(tokens, expert_ids, gate_probs, cotangent, weight_in, weight_down, swap_flag):
    row_count = tokens.shape[0]
    model_width = tokens.shape[1]
    per_device = weight_in.shape[0]
    groups = lax.axis_size("expert")
    experts = groups * per_device
    device_ids = jnp.arange(groups, dtype=jnp.int32)
    my_index = lax.axis_index("expert")
    my_flag = jnp.sum(jnp.where(device_ids == my_index, swap_flag, 0))
    expert_range = jnp.arange(experts, dtype=jnp.int32)
    chosen = expert_ids[:, :, None] == expert_range[None, None, :]
    member = jnp.any(chosen, axis=1)
    row_range = jnp.arange(row_count, dtype=jnp.int32)
    lower = (row_range[:, None] > row_range[None, :]).astype(jnp.bfloat16)
    earlier = jnp.dot(lower, member.astype(jnp.bfloat16), preferred_element_type=jnp.float32)
    rank = earlier.astype(jnp.int32)
    odd = (expert_range % 2 == 1)[None, :]
    rank = jnp.where(odd, CAP - 1 - rank, rank)
    slot_hit = member[:, :, None] & (rank[:, :, None] == jnp.arange(CAP, dtype=jnp.int32)[None, None, :])
    gather_rows = slot_hit.reshape(row_count, experts * CAP).astype(jnp.bfloat16)
    prob_of = jnp.sum(jnp.where(chosen, gate_probs[:, :, None], 0.0), axis=1)
    slot_prob = jnp.sum(jnp.where(slot_hit, prob_of[:, :, None], 0.0), axis=0).reshape(experts * CAP)
    send_x = jnp.dot(gather_rows.T, tokens, preferred_element_type=jnp.float32).astype(jnp.bfloat16)
    send_c = jnp.dot(gather_rows.T, cotangent, preferred_element_type=jnp.float32)
    send_grad = (slot_prob[:, None] * send_c).astype(jnp.bfloat16)
    lanes = per_device * CAP
    send_x = send_x.reshape(groups, lanes, model_width)
    send_grad = send_grad.reshape(groups, lanes, model_width)
    recv_x = lax.all_to_all(send_x, "expert", split_axis=0, concat_axis=0, tiled=True)
    recv_grad = lax.all_to_all(send_grad, "expert", split_axis=0, concat_axis=0, tiled=True)
    window = CAP + 4
    shift = lanes - window
    place = jnp.arange(window, dtype=jnp.int32)[None, :, None]
    forwards = []
    for local in range(per_device):
        low = local * shift
        rows_x = recv_x[:, low:low + window].reshape(groups * window, model_width)
        projected = jnp.dot(rows_x, weight_in[local], preferred_element_type=jnp.float32)
        pre_gate = projected[:, :FF]
        up_part = projected[:, FF:]
        sigmoid_gate = jax.nn.sigmoid(pre_gate)
        activated = pre_gate * sigmoid_gate
        hidden = (activated * up_part).astype(jnp.bfloat16)
        expert_out = jnp.dot(hidden, weight_down[local], preferred_element_type=jnp.float32).astype(
            jnp.bfloat16
        )
        forwards.append((rows_x, pre_gate, up_part, sigmoid_gate, activated, hidden, expert_out))

    def merged(pieces):
        tile = window - shift
        seam = jnp.arange(tile, dtype=jnp.int32)[None, :, None] < CAP - shift
        middle = jnp.where(seam, pieces[0][:, shift:], pieces[1][:, :tile])
        return jnp.concatenate([pieces[0][:, :shift], middle, pieces[1][:, tile:]], axis=1)

    send_out = merged([f[-1].reshape(groups, window, model_width) for f in forwards])
    send_out, recv_grad = lax.optimization_barrier((send_out, recv_grad))
    home_out = lax.all_to_all(send_out, "expert", split_axis=0, concat_axis=0, tiled=True)
    whole_grad = recv_grad.reshape(groups * lanes, model_width)
    lane = jnp.arange(lanes, dtype=jnp.int32)[None, :, None]
    seconds = []
    for local in range(per_device):
        low = local * shift
        hidden = forwards[local][5].reshape(groups, window, FF)
        padded = jnp.pad(hidden, ((0, 0), (low, lanes - window - low), (0, 0)))
        mine = (lane < CAP) if local == 0 else (lane >= CAP)
        padded = jnp.where(mine, padded, jnp.zeros((), jnp.bfloat16)).reshape(groups * lanes, FF)
        seconds.append(jnp.dot(padded.T, whole_grad, preferred_element_type=jnp.float32))
    grad_second = jnp.stack(seconds)
    recv_grad, grad_second = lax.optimization_barrier((recv_grad, grad_second))
    windows = []
    for local in range(per_device):
        low = local * shift
        own = (place < CAP) if local == 0 else (place >= window - CAP)
        rows_grad = jnp.where(own, recv_grad[:, low:low + window], jnp.zeros((), jnp.bfloat16))
        windows.append(rows_grad.reshape(groups * window, model_width))
    reduced_down = lax.psum_scatter(
        grad_second.astype(jnp.bfloat16), "dp", scatter_dimension=2, tiled=True
    )
    backs, firsts = [], []
    for local in range(per_device):
        rows_x, pre_gate, up_part, sigmoid_gate, activated, hidden, _ = forwards[local]
        rows_grad = windows[local]
        hidden_grad = jnp.dot(rows_grad, weight_down[local].T, preferred_element_type=jnp.float32)
        gate_grad = hidden_grad * up_part * sigmoid_gate * (1.0 + pre_gate * (1.0 - sigmoid_gate))
        proj_grad = jnp.concatenate([gate_grad, hidden_grad * activated], axis=-1).astype(
            jnp.bfloat16
        )
        row_grad = jnp.dot(proj_grad, weight_in[local].T, preferred_element_type=jnp.float32).astype(
            jnp.bfloat16
        )
        backs.append(row_grad.reshape(groups, window, model_width))
        firsts.append((rows_x, proj_grad))
    send_back, firsts, reduced_down = lax.optimization_barrier((merged(backs), firsts, reduced_down))
    firsts = [jnp.dot(a.T, b, preferred_element_type=jnp.float32) for a, b in firsts]
    grad_first, home_out = lax.optimization_barrier((jnp.stack(firsts), home_out))
    reduced_in = lax.psum_scatter(
        grad_first.astype(jnp.bfloat16), "dp", scatter_dimension=1, tiled=True
    )
    home_grad = lax.all_to_all(send_back, "expert", split_axis=0, concat_axis=0, tiled=True)
    partner_in, partner_down = swapped((reduced_in, reduced_down), "expert", 1)
    held_in = jnp.where(my_flag == 1, partner_in, reduced_in).astype(jnp.float32)
    held_down = jnp.where(my_flag == 1, partner_down, reduced_down).astype(jnp.float32)
    out_rows = home_out.reshape(experts * CAP, model_width)
    back_rows = home_grad.reshape(experts * CAP, model_width)
    combine = jnp.where(slot_hit, prob_of[:, :, None], 0.0).reshape(row_count, experts * CAP)
    layer_out = jnp.dot(
        combine, out_rows.astype(jnp.float32), precision=lax.Precision.HIGHEST,
        preferred_element_type=jnp.float32,
    ).astype(jnp.bfloat16)
    scores = jnp.dot(cotangent, out_rows.T, preferred_element_type=jnp.float32)
    rank_of = jnp.sum(jnp.where(chosen, rank[:, None, :], 0), axis=2)
    slot_of = expert_ids * CAP + rank_of
    gate_grads = jnp.take_along_axis(scores, slot_of, axis=1)
    token_grads = jnp.dot(gather_rows, back_rows, preferred_element_type=jnp.float32).astype(
        jnp.bfloat16
    )
    return (layer_out, gate_grads, token_grads, held_in, held_down)


def solution(mesh):
    in_specs = (
        P(("expert", "dp"), None),
        P(("expert", "dp"), None),
        P(("expert", "dp"), None),
        P(("expert", "dp"), None),
        P("expert", None, None),
        P("expert", None, None),
        P(),
    )
    out_specs = (
        P(("expert", "dp"), None),
        P(("expert", "dp"), None),
        P(("expert", "dp"), None),
        P("expert", "dp", None),
        P("expert", None, "dp"),
    )
    return jax.shard_map(body, mesh=mesh, in_specs=in_specs, out_specs=out_specs, check_vma=False)
```

```python
import jax
import jax.numpy as jnp
from jax import lax
from jax.sharding import PartitionSpec as P

FF = 384
TOP = 8
CAP = 20


def swapped(block, axis, apart):
    count = lax.axis_size(axis)
    route = []
    for low in range(count):
        high = low | 1 << apart
        if high != low and high < count:
            route += [(low, high), (high, low)]
    return lax.ppermute(block, axis, route)


def body(tokens, expert_ids, gate_probs, cotangent, weight_in, weight_down, swap_flag):
    row_count = tokens.shape[0]
    model_width = tokens.shape[1]
    per_device = weight_in.shape[0]
    groups = lax.axis_size("expert")
    experts = groups * per_device
    device_ids = jnp.arange(groups, dtype=jnp.int32)
    my_index = lax.axis_index("expert")
    my_flag = jnp.sum(jnp.where(device_ids == my_index, swap_flag, 0))
    expert_range = jnp.arange(experts, dtype=jnp.int32)
    chosen = expert_ids[:, :, None] == expert_range[None, None, :]
    member = jnp.any(chosen, axis=1)
    row_range = jnp.arange(row_count, dtype=jnp.int32)
    lower = (row_range[:, None] > row_range[None, :]).astype(jnp.bfloat16)
    earlier = jnp.dot(lower, member.astype(jnp.bfloat16), preferred_element_type=jnp.float32)
    rank = earlier.astype(jnp.int32)
    odd = (expert_range % 2 == 1)[None, :]
    rank = jnp.where(odd, CAP - 1 - rank, rank)
    slot_hit = member[:, :, None] & (rank[:, :, None] == jnp.arange(CAP, dtype=jnp.int32)[None, None, :])
    gather_rows = slot_hit.reshape(row_count, experts * CAP).astype(jnp.bfloat16)
    prob_of = jnp.sum(jnp.where(chosen, gate_probs[:, :, None], 0.0), axis=1)
    slot_prob = jnp.sum(jnp.where(slot_hit, prob_of[:, :, None], 0.0), axis=0).reshape(experts * CAP)
    send_x = jnp.dot(gather_rows.T, tokens, preferred_element_type=jnp.float32).astype(jnp.bfloat16)
    send_c = jnp.dot(gather_rows.T, cotangent, preferred_element_type=jnp.float32)
    send_grad = (slot_prob[:, None] * send_c).astype(jnp.bfloat16)
    lanes = per_device * CAP
    send_x = send_x.reshape(groups, lanes, model_width)
    send_grad = send_grad.reshape(groups, lanes, model_width)
    recv_x = lax.all_to_all(send_x, "expert", split_axis=0, concat_axis=0, tiled=True)
    recv_grad = lax.all_to_all(send_grad, "expert", split_axis=0, concat_axis=0, tiled=True)
    window = CAP + 4
    shift = lanes - window
    place = jnp.arange(window, dtype=jnp.int32)[None, :, None]
    forwards = []
    for local in range(per_device):
        low = local * shift
        rows_x = recv_x[:, low:low + window].reshape(groups * window, model_width)
        projected = jnp.dot(rows_x, weight_in[local], preferred_element_type=jnp.float32)
        pre_gate = projected[:, :FF]
        up_part = projected[:, FF:]
        sigmoid_gate = jax.nn.sigmoid(pre_gate)
        activated = pre_gate * sigmoid_gate
        hidden = (activated * up_part).astype(jnp.bfloat16)
        expert_out = jnp.dot(hidden, weight_down[local], preferred_element_type=jnp.float32).astype(
            jnp.bfloat16
        )
        forwards.append((rows_x, pre_gate, up_part, sigmoid_gate, activated, hidden, expert_out))

    def merged(pieces):
        tile = window - shift
        seam = jnp.arange(tile, dtype=jnp.int32)[None, :, None] < CAP - shift
        middle = jnp.where(seam, pieces[0][:, shift:], pieces[1][:, :tile])
        return jnp.concatenate([pieces[0][:, :shift], middle, pieces[1][:, tile:]], axis=1)

    send_out = merged([f[-1].reshape(groups, window, model_width) for f in forwards])
    send_out, recv_grad = lax.optimization_barrier((send_out, recv_grad))
    home_out = lax.all_to_all(send_out, "expert", split_axis=0, concat_axis=0, tiled=True)
    backs, firsts, seconds = [], [], []
    for local in range(per_device):
        low = local * shift
        rows_x, pre_gate, up_part, sigmoid_gate, activated, hidden, _ = forwards[local]
        own = (place < CAP) if local == 0 else (place >= window - CAP)
        rows_grad = jnp.where(own, recv_grad[:, low:low + window], jnp.zeros((), jnp.bfloat16))
        rows_grad = rows_grad.reshape(groups * window, model_width)
        hidden_grad = jnp.dot(rows_grad, weight_down[local].T, preferred_element_type=jnp.float32)
        gate_grad = hidden_grad * up_part * sigmoid_gate * (1.0 + pre_gate * (1.0 - sigmoid_gate))
        proj_grad = jnp.concatenate([gate_grad, hidden_grad * activated], axis=-1).astype(
            jnp.bfloat16
        )
        row_grad = jnp.dot(proj_grad, weight_in[local].T, preferred_element_type=jnp.float32).astype(
            jnp.bfloat16
        )
        backs.append(row_grad.reshape(groups, window, model_width))
        firsts.append((rows_x, proj_grad))
        seconds.append((hidden, rows_grad))
    send_back, firsts, seconds = lax.optimization_barrier((merged(backs), firsts, seconds))
    firsts = [jnp.dot(a.T, b, preferred_element_type=jnp.float32) for a, b in firsts]
    seconds = [jnp.dot(a.T, b, preferred_element_type=jnp.float32) for a, b in seconds]
    grad_first, grad_second, home_out = lax.optimization_barrier(
        (jnp.stack(firsts), jnp.stack(seconds), home_out)
    )
    reduced_in = lax.psum_scatter(
        grad_first.astype(jnp.bfloat16), "dp", scatter_dimension=1, tiled=True
    )
    reduced_down = lax.psum_scatter(
        grad_second.astype(jnp.bfloat16), "dp", scatter_dimension=2, tiled=True
    )
    home_grad = lax.all_to_all(send_back, "expert", split_axis=0, concat_axis=0, tiled=True)
    partner_in, partner_down = swapped((reduced_in, reduced_down), "expert", 1)
    held_in = jnp.where(my_flag == 1, partner_in, reduced_in).astype(jnp.float32)
    held_down = jnp.where(my_flag == 1, partner_down, reduced_down).astype(jnp.float32)
    out_rows = home_out.reshape(experts * CAP, model_width)
    back_rows = home_grad.reshape(experts * CAP, model_width)
    combine = jnp.where(slot_hit, prob_of[:, :, None], 0.0).reshape(row_count, experts * CAP)
    layer_out = jnp.dot(
        combine, out_rows.astype(jnp.float32), precision=lax.Precision.HIGHEST,
        preferred_element_type=jnp.float32,
    ).astype(jnp.bfloat16)
    scores = jnp.dot(cotangent, out_rows.T, preferred_element_type=jnp.float32)
    rank_of = jnp.sum(jnp.where(chosen, rank[:, None, :], 0), axis=2)
    slot_of = expert_ids * CAP + rank_of
    gate_grads = jnp.take_along_axis(scores, slot_of, axis=1)
    token_grads = jnp.dot(gather_rows, back_rows, preferred_element_type=jnp.float32).astype(
        jnp.bfloat16
    )
    return (layer_out, gate_grads, token_grads, held_in, held_down)


def solution(mesh):
    in_specs = (
        P(("expert", "dp"), None),
        P(("expert", "dp"), None),
        P(("expert", "dp"), None),
        P(("expert", "dp"), None),
        P("expert", None, None),
        P("expert", None, None),
        P(),
    )
    out_specs = (
        P(("expert", "dp"), None),
        P(("expert", "dp"), None),
        P(("expert", "dp"), None),
        P("expert", "dp", None),
        P("expert", None, "dp"),
    )
    return jax.shard_map(body, mesh=mesh, in_specs=in_specs, out_specs=out_specs, check_vma=False)
```
